32 devices in a mesh: img: 4 (over z), gx: 4 (over x, core), gy: 2 (over y).
Axes of the slice: x: 2, y: 2, z: 4, core: 2. Of those that a mesh axis runs over, the one named last changes fastest.
Arguments:
- spins: float32 [4, 3, 128, 128, 128], P('img', None, 'gx', 'gy'), may hold values from -1 to 1, as said below
- velocity: float32 [4, 3, 128, 128, 128], P('img', None, 'gx', 'gy'), may hold values from -3 to 3
- upwind: int32 [4], P('img'), may hold values from -1 to 1
- climber: int32 [1], replicated, may hold values from 1 to 2
- coupling: float32 [3], replicated, may hold values from 0.5 to 1.5
Outputs:
- new_spins: float32 [4, 3, 128, 128, 128], P('img', None, 'gx', 'gy')
- new_velocity: float32 [4, 3, 128, 128, 128], P('img', None, 'gx', 'gy')
- spacing: float32 [4, 2], P('img')
The draws below stay inside these ranges and needn't reach their ends.
Inputs may be any that keep to these rules, and one draw needn't show every extreme that they name: Every cell of spins is a unit vector.
All inputs are finite; a program needn't handle non-finite values.
Results may differ from the reference program's by a relative error of at most 0.0003.
Values sent between devices are 32-bit elements; how exact they have to be, the bound alone decides.
No kernel may reach another device: no remote copies, remote signals or barrier semaphores. Data moves between devices by JAX's collectives and lax.ppermute only.
A program may use at most 64 MiB of HBM per device.

```python
import jax
import jax.numpy as jnp
from jax import lax

NZ = 128
IMAGES = 4
NX = 128
NY = 128


def draw_spins(key, part):
    first_key, second_key = jax.random.split(jax.random.fold_in(key, 11))
    shared = jax.random.normal(first_key, (1, 3, NX, NY, NZ), jnp.float32)
    own = jax.random.normal(second_key, (IMAGES, 3, NX, NY, NZ), jnp.float32)
    along_path = jnp.arange(IMAGES, dtype=jnp.float32) / (IMAGES - 1)
    height = (2.5 - 5.0 * along_path * along_path).reshape(IMAGES, 1, 1, 1, 1)
    lift = jnp.array([0.0, 0.0, 1.0], jnp.float32).reshape(1, 3, 1, 1, 1)
    raw = shared + 0.15 * own + height * lift
    return raw / jnp.sqrt(jnp.sum(raw * raw, axis=1, keepdims=True))


def place_ends(drawn, rng, least, high):
    spot = [jax.random.randint(jax.random.fold_in(rng, axis), (), 0, length) for axis, length in enumerate(drawn.shape)]
    main_axis = drawn.shape.index(max(drawn.shape))
    beside = spot[:main_axis] + [(spot[main_axis] + 1) % drawn.shape[main_axis]] + spot[main_axis + 1:]
    return drawn.at[tuple(spot)].set(least).at[tuple(beside)].set(high)


def steps_of(rng, extent, pieces, low, largest):
    factor_of = 1.0
    for position, parts in pieces:
        heights = jax.random.uniform(jax.random.fold_in(jax.random.fold_in(rng, 6), position), (parts,), jnp.float32, low / len(pieces), largest / len(pieces))
        factor_of = factor_of * jnp.repeat(jnp.exp(heights), extent[position] // parts).reshape((-1,) + (1,) * (len(extent) - 1 - position))
    return factor_of


def normal_values(key, dims, width, limit, cuts=(), kind=jnp.bfloat16):
    loudness = steps_of(key, dims, cuts, -0.22, 0.18) if cuts else 1.0
    values = jax.random.normal(key, dims, jnp.float32) * width * loudness
    return jnp.minimum(jnp.maximum(values, -limit), limit).astype(kind)


def setup_inputs(seed: int = 0) -> dict:
    key_of = jax.random.split(jax.random.key(seed), 6)
    return {
        "spins": draw_spins(jax.random.fold_in(key_of[5], 71), 0),
        "velocity": normal_values(key_of[1], (IMAGES, 3, NX, NY, NZ), 0.5, 3.0, ((0, 4), (2, 4), (3, 2)), jnp.float32),
        "upwind": place_ends(jax.random.randint(key_of[2], (IMAGES,), -1, 2), jax.random.fold_in(key_of[2], 1), -1, 1).astype(jnp.int32),
        "climber": jax.random.randint(key_of[3], (1,), 1, IMAGES - 1).astype(jnp.int32),
        "coupling": jnp.clip(jax.random.uniform(key_of[4], (3,), jnp.float32, 0.5, 1.5), 0.5, 1.5),
    }


TIME_STEP = 0.1
SPRING = 2.0
EPSILON = 1e-06

def lattice_field(state, coupling):
    plus_x = jnp.roll(state, -1, 1)
    minus_x = jnp.roll(state, 1, 1)
    plus_y = jnp.roll(state, -1, 2)
    minus_y = jnp.roll(state, 1, 2)
    padded = jnp.pad(state, ((0, 0), (0, 0), (0, 0), (1, 1)))
    plus_z = padded[:, :, :, 2:]
    minus_z = padded[:, :, :, :-2]
    diff_x = plus_x - minus_x
    diff_y = plus_y - minus_y
    diff_z = plus_z - minus_z
    twist = jnp.stack([diff_y[2] - diff_z[1], diff_z[0] - diff_x[2], diff_x[1] - diff_y[0]], 0)
    neighbours = plus_x + minus_x + plus_y + minus_y + plus_z + minus_z
    lift = jnp.array([0.0, 0.0, 1.0], jnp.float32).reshape(3, 1, 1, 1)
    return coupling[0] * neighbours + coupling[1] * twist + coupling[2] * lift

def cell_dot(left, right):
    return lax.optimization_barrier(jnp.sum(left * right, axis=0, keepdims=True))

def reference(spins, velocity, upwind, climber, coupling):
    count = spins.shape[0]
    cells = spins.shape[2] * spins.shape[3] * spins.shape[4]
    root_cells = jnp.sqrt(jnp.asarray(cells, jnp.float32))
    zeros = jnp.zeros_like(spins[0])

    def one_image(index):
        state = spins[index]
        before = lax.dynamic_index_in_dim(spins, jnp.maximum(index - 1, 0).astype(jnp.int32), 0, False)
        after = lax.dynamic_index_in_dim(spins, jnp.minimum(index + 1, count - 1).astype(jnp.int32), 0, False)
        before = jnp.where(index == 0, zeros, before)
        after = jnp.where(index == count - 1, zeros, after)
        speed = velocity[index]
        field = lattice_field(state, coupling)
        perp_field = field - cell_dot(field, state) * state
        forward = after - state
        backward = state - before
        direction = upwind[index]
        raw = jnp.where(direction > 0, forward, jnp.where(direction < 0, backward, forward + backward))
        tangent_perp = raw - cell_dot(raw, state) * state
        norm_t = jnp.sum(tangent_perp * tangent_perp)
        dist_next = jnp.sqrt(jnp.sum(forward * forward) + EPSILON)
        dist_prev = jnp.sqrt(jnp.sum(backward * backward) + EPSILON)
        tau = tangent_perp / jnp.sqrt(norm_t + EPSILON)
        along = jnp.sum(perp_field * tau)
        climbing = index == climber[0]
        ending = (index == 0) | (index == count - 1)
        weight = jnp.where(climbing, 2.0 * along, along - SPRING * (dist_next - dist_prev))
        force = perp_field - weight * tau
        force = jnp.where(ending, jnp.zeros_like(force), force)
        projected = jnp.maximum(cell_dot(speed, force), 0.0) / jnp.maximum(cell_dot(force, force), 1.0) * force
        speed_new = projected + TIME_STEP * force
        moved = state + TIME_STEP * speed_new
        gaps = jnp.stack([dist_next, dist_prev]) / root_cells
        return (moved / jnp.sqrt(cell_dot(moved, moved)), speed_new, gaps)
    new_spins, new_velocity, spacing = lax.map(one_image, jnp.arange(count, dtype=jnp.int32))
    return (new_spins, new_velocity, spacing)
```

```python
import jax
import jax.numpy as jnp
from jax import lax
from jax.sharding import PartitionSpec as P

TIME_STEP = 0.1
SPRING = 2.0
EPSILON = 1e-06


def extended(block, sides, width):
    for axis, dim in sides:
        count = lax.axis_size(axis)
        forward = [(i, i + 1) for i in range(count - 1)]
        forward.append((count - 1, 0))
        backward = [(target, source) for source, target in forward]
        low = lax.ppermute(
            lax.slice_in_dim(block, block.shape[dim] - width, None, axis=dim), axis, forward
        )
        high = lax.ppermute(lax.slice_in_dim(block, 0, width, axis=dim), axis, backward)
        block = jnp.concatenate([low, block, high], axis=dim)
    return block


def from_behind(value, axis, by):
    size = lax.axis_size(axis)
    pairs = [(i, i + by) for i in range(size) if 0 <= i + by < size]
    return lax.ppermute(value, axis, pairs)


def group_sum(value, axes):
    for axis in axes:
        size = lax.axis_size(axis)
        if size & (size - 1):
            value = lax.psum(value, axis)
            continue
        step = 1
        while step < size:
            pairs = [(i, i ^ step) for i in range(size)]
            value = value + lax.ppermute(value, axis, pairs)
            step *= 2
    return value


def cell_dot(left, right):
    return jnp.sum(left * right, axis=1, keepdims=True)


def lattice_field(state, coupling):
    padded = extended(state, (("gx", 2), ("gy", 3)), 1)
    plus_x = padded[:, :, 2:, 1:-1]
    minus_x = padded[:, :, :-2, 1:-1]
    plus_y = padded[:, :, 1:-1, 2:]
    minus_y = padded[:, :, 1:-1, :-2]
    zpadded = jnp.pad(state, ((0, 0), (0, 0), (0, 0), (0, 0), (1, 1)))
    plus_z = zpadded[..., 2:]
    minus_z = zpadded[..., :-2]
    diff_x = plus_x - minus_x
    diff_y = plus_y - minus_y
    diff_z = plus_z - minus_z
    twist = jnp.stack(
        [diff_y[:, 2] - diff_z[:, 1], diff_z[:, 0] - diff_x[:, 2], diff_x[:, 1] - diff_y[:, 0]], 1
    )
    neighbours = plus_x + minus_x + plus_y + minus_y + plus_z + minus_z
    lift = jnp.array([0.0, 0.0, 1.0], jnp.float32).reshape(1, 3, 1, 1, 1)
    return coupling[0] * neighbours + coupling[1] * twist + coupling[2] * lift


def per_device(spins, velocity, upwind, climber, coupling):
    count = spins.shape[0]
    total = count * lax.axis_size("img")
    cells = (
        spins.shape[2] * spins.shape[3] * spins.shape[4] * lax.axis_size("gx") * lax.axis_size("gy")
    )
    root_cells = jnp.sqrt(jnp.asarray(cells, jnp.float32))
    indices = lax.axis_index("img") * count + jnp.arange(count, dtype=jnp.int32)
    axes_all = (1, 2, 3, 4)
    ahead = from_behind(spins[:1], "img", -1)
    behind = from_behind(spins[-1:], "img", 1)
    field = lattice_field(spins, coupling)
    perp_field = field - cell_dot(field, spins) * spins
    after = jnp.concatenate([spins[1:], ahead], 0)
    before = jnp.concatenate([behind, spins[:-1]], 0)
    forward = after - spins
    backward = spins - before
    direction = upwind.reshape(count, 1, 1, 1, 1)
    raw = jnp.where(direction > 0, forward, jnp.where(direction < 0, backward, forward + backward))
    tangent_perp = raw - cell_dot(raw, spins) * spins
    parts = jnp.stack(
        [
            jnp.sum(tangent_perp * tangent_perp, axis=axes_all),
            jnp.sum(perp_field * tangent_perp, axis=axes_all),
            jnp.sum(forward * forward, axis=axes_all),
            jnp.sum(backward * backward, axis=axes_all),
        ],
        1,
    )
    norm_t, along_t, next_sq, prev_sq = jnp.moveaxis(group_sum(parts, ("gy", "gx")), 1, 0)
    scale = 1.0 / jnp.sqrt(norm_t + EPSILON)
    along = along_t * scale
    dist_next = jnp.sqrt(next_sq + EPSILON)
    dist_prev = jnp.sqrt(prev_sq + EPSILON)
    spacing = jnp.stack([dist_next, dist_prev], 1) / root_cells
    climbing = indices == climber[0]
    ending = (indices == 0) | (indices == total - 1)
    weight = jnp.where(climbing, 2.0 * along, along - SPRING * (dist_next - dist_prev))
    weight = jnp.where(ending, 0.0, weight * scale)
    keep = jnp.where(ending, 0.0, 1.0).reshape(count, 1, 1, 1, 1)
    force = keep * perp_field - weight.reshape(count, 1, 1, 1, 1) * tangent_perp
    projected = (
        jnp.maximum(cell_dot(velocity, force), 0.0)
        / jnp.maximum(cell_dot(force, force), 1.0)
        * force
    )
    speed_new = projected + TIME_STEP * force
    moved = spins + TIME_STEP * speed_new
    return (moved / jnp.sqrt(cell_dot(moved, moved)), speed_new, spacing)


def solution(mesh):
    return jax.shard_map(
        per_device,
        mesh=mesh,
        in_specs=(
            P("img", None, "gx", "gy", None),
            P("img", None, "gx", "gy", None),
            P("img"),
            P(),
            P(),
        ),
        out_specs=(
            P("img", None, "gx", "gy", None),
            P("img", None, "gx", "gy", None),
            P("img", None),
        ),
        check_vma=False,
    )
```

```python
import functools

import jax
import jax.numpy as jnp
from jax import lax
from jax.experimental import pallas as pl
from jax.experimental.pallas import tpu as pltpu
from jax.sharding import PartitionSpec as P

TIME_STEP = 0.1
SPRING = 2.0
EPSILON = 1e-06
ROWS = 4


def extended(block, sides, width):
    for axis, dim in sides:
        count = lax.axis_size(axis)
        forward = [(i, i + 1) for i in range(count - 1)]
        forward.append((count - 1, 0))
        backward = [(target, source) for source, target in forward]
        low = lax.ppermute(
            lax.slice_in_dim(block, block.shape[dim] - width, None, axis=dim), axis, forward
        )
        high = lax.ppermute(lax.slice_in_dim(block, 0, width, axis=dim), axis, backward)
        block = jnp.concatenate([low, block, high], axis=dim)
    return block


def from_behind(value, axis, by):
    size = lax.axis_size(axis)
    pairs = [(i, i + by) for i in range(size) if 0 <= i + by < size]
    return lax.ppermute(value, axis, pairs)


def group_sum(value, axes):
    for axis in axes:
        size = lax.axis_size(axis)
        if size & (size - 1):
            value = lax.psum(value, axis)
            continue
        step = 1
        while step < size:
            pairs = [(i, i ^ step) for i in range(size)]
            value = value + lax.ppermute(value, axis, pairs)
            step *= 2
    return value


def cell_dot(left, right):
    return jnp.sum(left * right, axis=1, keepdims=True)


def lattice_field(state, coupling):
    padded = extended(state, (("gx", 2), ("gy", 3)), 1)
    plus_x = padded[:, :, 2:, 1:-1]
    minus_x = padded[:, :, :-2, 1:-1]
    plus_y = padded[:, :, 1:-1, 2:]
    minus_y = padded[:, :, 1:-1, :-2]
    zpadded = jnp.pad(state, ((0, 0), (0, 0), (0, 0), (0, 0), (1, 1)))
    plus_z = zpadded[..., 2:]
    minus_z = zpadded[..., :-2]
    diff_x = plus_x - minus_x
    diff_y = plus_y - minus_y
    diff_z = plus_z - minus_z
    twist = jnp.stack(
        [diff_y[:, 2] - diff_z[:, 1], diff_z[:, 0] - diff_x[:, 2], diff_x[:, 1] - diff_y[:, 0]], 1
    )
    neighbours = plus_x + minus_x + plus_y + minus_y + plus_z + minus_z
    lift = jnp.array([0.0, 0.0, 1.0], jnp.float32).reshape(1, 3, 1, 1, 1)
    return coupling[0] * neighbours + coupling[1] * twist + coupling[2] * lift


def fold(x):
    return jnp.sum(x.reshape(-1, 8, x.shape[-1]), axis=0)


def tangent_kernel(up_ref, s_ref, nx_ref, pv_ref, pf_ref, tp_ref, sums_ref, acc_ref):
    step = pl.program_id(1)

    @pl.when(step == 0)
    def _():
        acc_ref[...] = jnp.zeros_like(acc_ref)

    up = up_ref[pl.program_id(0)]
    ahead = jnp.where(up >= 0, 1.0, 0.0).astype(jnp.float32)
    behind = jnp.where(up <= 0, 1.0, 0.0).astype(jnp.float32)
    s = [s_ref[0, c] for c in range(3)]
    fwd = [nx_ref[0, c] - s[c] for c in range(3)]
    bwd = [s[c] - pv_ref[0, c] for c in range(3)]
    raw = [ahead * fwd[c] + behind * bwd[c] for c in range(3)]
    d = raw[0] * s[0] + raw[1] * s[1] + raw[2] * s[2]
    tp = [raw[c] - d * s[c] for c in range(3)]
    for c in range(3):
        tp_ref[0, c] = tp[c]
    pf = [pf_ref[0, c] for c in range(3)]
    acc_ref[0] += fold(tp[0] * tp[0] + tp[1] * tp[1] + tp[2] * tp[2])
    acc_ref[1] += fold(pf[0] * tp[0] + pf[1] * tp[1] + pf[2] * tp[2])
    acc_ref[2] += fold(fwd[0] * fwd[0] + fwd[1] * fwd[1] + fwd[2] * fwd[2])
    acc_ref[3] += fold(bwd[0] * bwd[0] + bwd[1] * bwd[1] + bwd[2] * bwd[2])

    @pl.when(step == pl.num_programs(1) - 1)
    def _():
        lane = lax.broadcasted_iota(jnp.int32, (8, 128), 1)
        row = lax.broadcasted_iota(jnp.int32, (8, 128), 0)
        out = jnp.zeros((8, 128), jnp.float32)
        for k in range(4):
            total = jnp.sum(acc_ref[k], keepdims=True)
            out = jnp.where((row == 0) & (lane == k), total, out)
        sums_ref[0] = out


def update_kernel(root_cells, flag_ref, sums_ref, s_ref, v_ref, pf_ref, tp_ref, ns_ref, nv_ref, sp_ref):
    image = pl.program_id(0)
    tot = sums_ref[0]
    lane = lax.broadcasted_iota(jnp.int32, (8, 128), 1)
    row = lax.broadcasted_iota(jnp.int32, (8, 128), 0)

    def pick(k):
        return jnp.sum(jnp.where((row == 0) & (lane == k), tot, 0.0), keepdims=True)

    norm_t, along_t, next_sq, prev_sq = (pick(k) for k in range(4))
    scale = 1.0 / jnp.sqrt(norm_t + EPSILON)
    along = along_t * scale
    dist_next = jnp.sqrt(next_sq + EPSILON)
    dist_prev = jnp.sqrt(prev_sq + EPSILON)
    climbing = jnp.full((1, 1), flag_ref[0, image]) > 0
    ending = jnp.full((1, 1), flag_ref[1, image]) > 0
    weight = jnp.where(climbing, 2.0 * along, along - SPRING * (dist_next - dist_prev))
    coef = jnp.where(ending, 0.0, weight * scale)
    keep = jnp.where(ending, 0.0, 1.0)

    @pl.when(pl.program_id(1) == 0)
    def _():
        pair = lax.broadcasted_iota(jnp.int32, (1, 2), 1)
        sp_ref[0] = jnp.where(pair == 0, dist_next, dist_prev) / root_cells

    f = [keep * pf_ref[0, c] - coef * tp_ref[0, c] for c in range(3)]
    v = [v_ref[0, c] for c in range(3)]
    vf = v[0] * f[0] + v[1] * f[1] + v[2] * f[2]
    ff = f[0] * f[0] + f[1] * f[1] + f[2] * f[2]
    gain = jnp.maximum(vf, 0.0) / jnp.maximum(ff, 1.0)
    nv = [gain * f[c] + TIME_STEP * f[c] for c in range(3)]
    moved = [s_ref[0, c] + TIME_STEP * nv[c] for c in range(3)]
    length = jnp.sqrt(moved[0] * moved[0] + moved[1] * moved[1] + moved[2] * moved[2])
    for c in range(3):
        nv_ref[0, c] = nv[c]
        ns_ref[0, c] = moved[c] / length


def per_device(spins, velocity, upwind, climber, coupling):
    count, _, nx, ny, nz = spins.shape
    total = count * lax.axis_size("img")
    cells = nx * ny * nz * lax.axis_size("gx") * lax.axis_size("gy")
    root_cells = float(cells) ** 0.5
    indices = lax.axis_index("img") * count + jnp.arange(count, dtype=jnp.int32)
    ahead = from_behind(spins[:1], "img", -1)
    behind = from_behind(spins[-1:], "img", 1)
    field = lattice_field(spins, coupling)
    perp_field = field - cell_dot(field, spins) * spins
    after = jnp.concatenate([spins[1:], ahead], 0)
    before = jnp.concatenate([behind, spins[:-1]], 0)

    rows = ROWS if nx % ROWS == 0 else nx
    grid = (count, nx // rows)
    block = pl.BlockSpec((1, 3, rows, ny, nz), lambda i, j: (i, 0, j, 0, 0))
    small = pl.BlockSpec((1, 8, 128), lambda i, j: (i, 0, 0))
    smem = pl.BlockSpec(memory_space=pltpu.SMEM)
    big = jax.ShapeDtypeStruct(spins.shape, jnp.float32)
    nbytes = spins.size * 4
    tangent_perp, sums = pl.pallas_call(
        tangent_kernel,
        grid=grid,
        in_specs=[smem, block, block, block, block],
        out_specs=[block, small],
        out_shape=[big, jax.ShapeDtypeStruct((count, 8, 128), jnp.float32)],
        scratch_shapes=[pltpu.VMEM((4, 8, nz), jnp.float32)],
        compiler_params=pltpu.CompilerParams(dimension_semantics=("arbitrary", "arbitrary")),
        cost_estimate=pl.CostEstimate(flops=40 * spins.size, bytes_accessed=5 * nbytes, transcendentals=0),
    )(upwind, spins, after, before, perp_field)

    sums = group_sum(sums, ("gy", "gx"))
    climbing = indices == climber[0]
    ending = (indices == 0) | (indices == total - 1)
    flags = jnp.stack([climbing, ending], 0).astype(jnp.int32)
    new_spins, new_velocity, spacing = pl.pallas_call(
        functools.partial(update_kernel, root_cells),
        grid=grid,
        in_specs=[smem, small, block, block, block, block],
        out_specs=[block, block, pl.BlockSpec((1, 1, 2), lambda i, j: (i, 0, 0))],
        out_shape=[big, big, jax.ShapeDtypeStruct((count, 1, 2), jnp.float32)],
        compiler_params=pltpu.CompilerParams(dimension_semantics=("arbitrary", "arbitrary")),
        cost_estimate=pl.CostEstimate(flops=45 * spins.size, bytes_accessed=6 * nbytes, transcendentals=spins.size // 3),
    )(flags, sums, spins, velocity, perp_field, tangent_perp)
    return new_spins, new_velocity, spacing.reshape(count, 2)


def solution(mesh):
    return jax.shard_map(
        per_device,
        mesh=mesh,
        in_specs=(
            P("img", None, "gx", "gy", None),
            P("img", None, "gx", "gy", None),
            P("img"),
            P(),
            P(),
        ),
        out_specs=(
            P("img", None, "gx", "gy", None),
            P("img", None, "gx", "gy", None),
            P("img", None),
        ),
        check_vma=False,
    )
```

```python
import functools

import jax
import jax.numpy as jnp
from jax import lax
from jax.experimental import pallas as pl
from jax.experimental.pallas import tpu as pltpu
from jax.sharding import PartitionSpec as P

TIME_STEP = 0.1
SPRING = 2.0
EPSILON = 1e-06
ROWS = 4


def extended(block, sides, width):
    for axis, dim in sides:
        count = lax.axis_size(axis)
        forward = [(i, i + 1) for i in range(count - 1)]
        forward.append((count - 1, 0))
        backward = [(target, source) for source, target in forward]
        low = lax.ppermute(
            lax.slice_in_dim(block, block.shape[dim] - width, None, axis=dim), axis, forward
        )
        high = lax.ppermute(lax.slice_in_dim(block, 0, width, axis=dim), axis, backward)
        block = jnp.concatenate([low, block, high], axis=dim)
    return block


def from_behind(value, axis, by):
    size = lax.axis_size(axis)
    pairs = [(i, i + by) for i in range(size) if 0 <= i + by < size]
    return lax.ppermute(value, axis, pairs)


def group_sum(value, axes):
    size = 1
    for axis in axes:
        size *= lax.axis_size(axis)
    me = lax.axis_index(axes)
    held = [value]
    for shift in range(size - 1, 0, -1):
        pairs = [(i, (i + shift) % size) for i in range(size)]
        held.append(lax.ppermute(value, axes, pairs))
    ordered = jnp.roll(jnp.stack(held, 0), me, axis=0)
    total = ordered[0]
    for m in range(1, size):
        total = total + ordered[m]
    return total


def cell_dot(left, right):
    return jnp.sum(left * right, axis=1, keepdims=True)


def lattice_field(state, coupling):
    padded = extended(state, (("gx", 2), ("gy", 3)), 1)
    plus_x = padded[:, :, 2:, 1:-1]
    minus_x = padded[:, :, :-2, 1:-1]
    plus_y = padded[:, :, 1:-1, 2:]
    minus_y = padded[:, :, 1:-1, :-2]
    zpadded = jnp.pad(state, ((0, 0), (0, 0), (0, 0), (0, 0), (1, 1)))
    plus_z = zpadded[..., 2:]
    minus_z = zpadded[..., :-2]
    diff_x = plus_x - minus_x
    diff_y = plus_y - minus_y
    diff_z = plus_z - minus_z
    twist = jnp.stack(
        [diff_y[:, 2] - diff_z[:, 1], diff_z[:, 0] - diff_x[:, 2], diff_x[:, 1] - diff_y[:, 0]], 1
    )
    neighbours = plus_x + minus_x + plus_y + minus_y + plus_z + minus_z
    lift = jnp.array([0.0, 0.0, 1.0], jnp.float32).reshape(1, 3, 1, 1, 1)
    return coupling[0] * neighbours + coupling[1] * twist + coupling[2] * lift


def fold(x):
    return jnp.sum(x.reshape(-1, 8, x.shape[-1]), axis=0)


def tangent_kernel(up_ref, s_ref, nx_ref, pv_ref, pf_ref, tp_ref, sums_ref, acc_ref):
    step = pl.program_id(1)

    @pl.when(step == 0)
    def _():
        acc_ref[...] = jnp.zeros_like(acc_ref)

    up = up_ref[pl.program_id(0)]
    ahead = jnp.where(up >= 0, 1.0, 0.0).astype(jnp.float32)
    behind = jnp.where(up <= 0, 1.0, 0.0).astype(jnp.float32)
    s = [s_ref[0, c] for c in range(3)]
    fwd = [nx_ref[0, c] - s[c] for c in range(3)]
    bwd = [s[c] - pv_ref[0, c] for c in range(3)]
    raw = [ahead * fwd[c] + behind * bwd[c] for c in range(3)]
    d = raw[0] * s[0] + raw[1] * s[1] + raw[2] * s[2]
    tp = [raw[c] - d * s[c] for c in range(3)]
    for c in range(3):
        tp_ref[0, c] = tp[c]
    pf = [pf_ref[0, c] for c in range(3)]
    acc_ref[0] += fold(tp[0] * tp[0] + tp[1] * tp[1] + tp[2] * tp[2])
    acc_ref[1] += fold(pf[0] * tp[0] + pf[1] * tp[1] + pf[2] * tp[2])
    acc_ref[2] += fold(fwd[0] * fwd[0] + fwd[1] * fwd[1] + fwd[2] * fwd[2])
    acc_ref[3] += fold(bwd[0] * bwd[0] + bwd[1] * bwd[1] + bwd[2] * bwd[2])

    @pl.when(step == pl.num_programs(1) - 1)
    def _():
        lane = lax.broadcasted_iota(jnp.int32, (8, 128), 1)
        row = lax.broadcasted_iota(jnp.int32, (8, 128), 0)
        out = jnp.zeros((8, 128), jnp.float32)
        for k in range(4):
            total = jnp.sum(acc_ref[k], keepdims=True)
            out = jnp.where((row == 0) & (lane == k), total, out)
        sums_ref[0] = out


def update_kernel(root_cells, flag_ref, sums_ref, s_ref, v_ref, pf_ref, tp_ref, ns_ref, nv_ref, sp_ref):
    image = pl.program_id(0)
    tot = sums_ref[0]
    lane = lax.broadcasted_iota(jnp.int32, (8, 128), 1)
    row = lax.broadcasted_iota(jnp.int32, (8, 128), 0)

    def pick(k):
        return jnp.sum(jnp.where((row == 0) & (lane == k), tot, 0.0), keepdims=True)

    norm_t, along_t, next_sq, prev_sq = (pick(k) for k in range(4))
    scale = 1.0 / jnp.sqrt(norm_t + EPSILON)
    along = along_t * scale
    dist_next = jnp.sqrt(next_sq + EPSILON)
    dist_prev = jnp.sqrt(prev_sq + EPSILON)
    climbing = jnp.full((1, 1), flag_ref[0, image]) > 0
    ending = jnp.full((1, 1), flag_ref[1, image]) > 0
    weight = jnp.where(climbing, 2.0 * along, along - SPRING * (dist_next - dist_prev))
    coef = jnp.where(ending, 0.0, weight * scale)
    keep = jnp.where(ending, 0.0, 1.0)

    @pl.when(pl.program_id(1) == 0)
    def _():
        pair = lax.broadcasted_iota(jnp.int32, (1, 2), 1)
        sp_ref[0] = jnp.where(pair == 0, dist_next, dist_prev) / root_cells

    f = [keep * pf_ref[0, c] - coef * tp_ref[0, c] for c in range(3)]
    v = [v_ref[0, c] for c in range(3)]
    vf = v[0] * f[0] + v[1] * f[1] + v[2] * f[2]
    ff = f[0] * f[0] + f[1] * f[1] + f[2] * f[2]
    gain = jnp.maximum(vf, 0.0) / jnp.maximum(ff, 1.0)
    nv = [gain * f[c] + TIME_STEP * f[c] for c in range(3)]
    moved = [s_ref[0, c] + TIME_STEP * nv[c] for c in range(3)]
    length = jnp.sqrt(moved[0] * moved[0] + moved[1] * moved[1] + moved[2] * moved[2])
    for c in range(3):
        nv_ref[0, c] = nv[c]
        ns_ref[0, c] = moved[c] / length


def per_device(spins, velocity, upwind, climber, coupling):
    count, _, nx, ny, nz = spins.shape
    total = count * lax.axis_size("img")
    cells = nx * ny * nz * lax.axis_size("gx") * lax.axis_size("gy")
    root_cells = float(cells) ** 0.5
    indices = lax.axis_index("img") * count + jnp.arange(count, dtype=jnp.int32)
    ahead = from_behind(spins[:1], "img", -1)
    behind = from_behind(spins[-1:], "img", 1)
    field = lattice_field(spins, coupling)
    perp_field = field - cell_dot(field, spins) * spins
    after = jnp.concatenate([spins[1:], ahead], 0)
    before = jnp.concatenate([behind, spins[:-1]], 0)

    rows = ROWS if nx % ROWS == 0 else nx
    grid = (count, nx // rows)
    block = pl.BlockSpec((1, 3, rows, ny, nz), lambda i, j: (i, 0, j, 0, 0))
    small = pl.BlockSpec((1, 8, 128), lambda i, j: (i, 0, 0))
    smem = pl.BlockSpec(memory_space=pltpu.SMEM)
    big = jax.ShapeDtypeStruct(spins.shape, jnp.float32)
    nbytes = spins.size * 4
    tangent_perp, sums = pl.pallas_call(
        tangent_kernel,
        grid=grid,
        in_specs=[smem, block, block, block, block],
        out_specs=[block, small],
        out_shape=[big, jax.ShapeDtypeStruct((count, 8, 128), jnp.float32)],
        scratch_shapes=[pltpu.VMEM((4, 8, nz), jnp.float32)],
        compiler_params=pltpu.CompilerParams(dimension_semantics=("arbitrary", "arbitrary")),
        cost_estimate=pl.CostEstimate(flops=40 * spins.size, bytes_accessed=5 * nbytes, transcendentals=0),
    )(upwind, spins, after, before, perp_field)

    sums = group_sum(sums, ("gx", "gy"))
    climbing = indices == climber[0]
    ending = (indices == 0) | (indices == total - 1)
    flags = jnp.stack([climbing, ending], 0).astype(jnp.int32)
    new_spins, new_velocity, spacing = pl.pallas_call(
        functools.partial(update_kernel, root_cells),
        grid=grid,
        in_specs=[smem, small, block, block, block, block],
        out_specs=[block, block, pl.BlockSpec((1, 1, 2), lambda i, j: (i, 0, 0))],
        out_shape=[big, big, jax.ShapeDtypeStruct((count, 1, 2), jnp.float32)],
        compiler_params=pltpu.CompilerParams(dimension_semantics=("arbitrary", "arbitrary")),
        cost_estimate=pl.CostEstimate(flops=45 * spins.size, bytes_accessed=6 * nbytes, transcendentals=spins.size // 3),
    )(flags, sums, spins, velocity, perp_field, tangent_perp)
    return new_spins, new_velocity, spacing.reshape(count, 2)


def solution(mesh):
    return jax.shard_map(
        per_device,
        mesh=mesh,
        in_specs=(
            P("img", None, "gx", "gy", None),
            P("img", None, "gx", "gy", None),
            P("img"),
            P(),
            P(),
        ),
        out_specs=(
            P("img", None, "gx", "gy", None),
            P("img", None, "gx", "gy", None),
            P("img", None),
        ),
        check_vma=False,
    )
```

```python
import functools

import jax
import jax.numpy as jnp
from jax import lax
from jax.experimental import pallas as pl
from jax.experimental.pallas import tpu as pltpu
from jax.sharding import PartitionSpec as P

TIME_STEP = 0.1
SPRING = 2.0
EPSILON = 1e-06
ROWS = 4
VMEM_LIMIT = 8 * 1024 * 1024


def extended(block, sides, width):
    for axis, dim in sides:
        count = lax.axis_size(axis)
        forward = [(i, i + 1) for i in range(count - 1)]
        forward.append((count - 1, 0))
        backward = [(target, source) for source, target in forward]
        low = lax.ppermute(
            lax.slice_in_dim(block, block.shape[dim] - width, None, axis=dim), axis, forward
        )
        high = lax.ppermute(lax.slice_in_dim(block, 0, width, axis=dim), axis, backward)
        block = jnp.concatenate([low, block, high], axis=dim)
    return block


def from_behind(value, axis, by):
    size = lax.axis_size(axis)
    pairs = [(i, i + by) for i in range(size) if 0 <= i + by < size]
    return lax.ppermute(value, axis, pairs)


def group_sum(value, axes):
    for axis in axes:
        size = lax.axis_size(axis)
        if size & (size - 1):
            value = lax.psum(value, axis)
            continue
        step = 1
        while step < size:
            pairs = [(i, i ^ step) for i in range(size)]
            value = value + lax.ppermute(value, axis, pairs)
            step *= 2
    return value


def cell_dot(left, right):
    return jnp.sum(left * right, axis=1, keepdims=True)


def lattice_field(state, coupling):
    padded = extended(state, (("gx", 2), ("gy", 3)), 1)
    plus_x = padded[:, :, 2:, 1:-1]
    minus_x = padded[:, :, :-2, 1:-1]
    plus_y = padded[:, :, 1:-1, 2:]
    minus_y = padded[:, :, 1:-1, :-2]
    zpadded = jnp.pad(state, ((0, 0), (0, 0), (0, 0), (0, 0), (1, 1)))
    plus_z = zpadded[..., 2:]
    minus_z = zpadded[..., :-2]
    diff_x = plus_x - minus_x
    diff_y = plus_y - minus_y
    diff_z = plus_z - minus_z
    twist = jnp.stack(
        [diff_y[:, 2] - diff_z[:, 1], diff_z[:, 0] - diff_x[:, 2], diff_x[:, 1] - diff_y[:, 0]], 1
    )
    neighbours = plus_x + minus_x + plus_y + minus_y + plus_z + minus_z
    lift = jnp.array([0.0, 0.0, 1.0], jnp.float32).reshape(1, 3, 1, 1, 1)
    return coupling[0] * neighbours + coupling[1] * twist + coupling[2] * lift


def fold(x):
    return jnp.sum(x.reshape(-1, 8, x.shape[-1]), axis=0)


def tangent_kernel(rows, up_ref, s_ref, nx_ref, pv_ref, pf_ref, tp_ref, sums_ref, acc_ref):
    image = pl.program_id(0)
    step = pl.program_id(1)
    here = pl.ds(pl.multiple_of(step * rows, rows), rows)

    @pl.when(step == 0)
    def _():
        acc_ref[...] = jnp.zeros_like(acc_ref)

    up = up_ref[pl.program_id(0)]
    ahead = jnp.where(up >= 0, 1.0, 0.0).astype(jnp.float32)
    behind = jnp.where(up <= 0, 1.0, 0.0).astype(jnp.float32)
    s = [s_ref[image, c, here] for c in range(3)]
    fwd = [nx_ref[0, c] - s[c] for c in range(3)]
    bwd = [s[c] - pv_ref[0, c] for c in range(3)]
    raw = [ahead * fwd[c] + behind * bwd[c] for c in range(3)]
    d = raw[0] * s[0] + raw[1] * s[1] + raw[2] * s[2]
    tp = [raw[c] - d * s[c] for c in range(3)]
    for c in range(3):
        tp_ref[image, c, here] = tp[c]
    pf = [pf_ref[image, c, here] for c in range(3)]
    acc_ref[0] += fold(tp[0] * tp[0] + tp[1] * tp[1] + tp[2] * tp[2])
    acc_ref[1] += fold(pf[0] * tp[0] + pf[1] * tp[1] + pf[2] * tp[2])
    acc_ref[2] += fold(fwd[0] * fwd[0] + fwd[1] * fwd[1] + fwd[2] * fwd[2])
    acc_ref[3] += fold(bwd[0] * bwd[0] + bwd[1] * bwd[1] + bwd[2] * bwd[2])

    @pl.when(step == pl.num_programs(1) - 1)
    def _():
        lane = lax.broadcasted_iota(jnp.int32, (8, 128), 1)
        row = lax.broadcasted_iota(jnp.int32, (8, 128), 0)
        out = jnp.zeros((8, 128), jnp.float32)
        for k in range(4):
            total = jnp.sum(acc_ref[k], keepdims=True)
            out = jnp.where((row == 0) & (lane == k), total, out)
        sums_ref[0] = out


def update_kernel(root_cells, rows, flag_ref, sums_ref, s_ref, v_ref, pf_ref, tp_ref, ns_ref, nv_ref, sp_ref):
    image = pl.program_id(0)
    here = pl.ds(pl.multiple_of(pl.program_id(1) * rows, rows), rows)
    tot = sums_ref[0]
    lane = lax.broadcasted_iota(jnp.int32, (8, 128), 1)
    row = lax.broadcasted_iota(jnp.int32, (8, 128), 0)

    def pick(k):
        return jnp.sum(jnp.where((row == 0) & (lane == k), tot, 0.0), keepdims=True)

    norm_t, along_t, next_sq, prev_sq = (pick(k) for k in range(4))
    scale = 1.0 / jnp.sqrt(norm_t + EPSILON)
    along = along_t * scale
    dist_next = jnp.sqrt(next_sq + EPSILON)
    dist_prev = jnp.sqrt(prev_sq + EPSILON)
    climbing = jnp.full((1, 1), flag_ref[0, image]) > 0
    ending = jnp.full((1, 1), flag_ref[1, image]) > 0
    weight = jnp.where(climbing, 2.0 * along, along - SPRING * (dist_next - dist_prev))
    coef = jnp.where(ending, 0.0, weight * scale)
    keep = jnp.where(ending, 0.0, 1.0)

    @pl.when(pl.program_id(1) == 0)
    def _():
        pair = lax.broadcasted_iota(jnp.int32, (1, 2), 1)
        sp_ref[0] = jnp.where(pair == 0, dist_next, dist_prev) / root_cells

    f = [keep * pf_ref[image, c, here] - coef * tp_ref[image, c, here] for c in range(3)]
    v = [v_ref[image, c, here] for c in range(3)]
    vf = v[0] * f[0] + v[1] * f[1] + v[2] * f[2]
    ff = f[0] * f[0] + f[1] * f[1] + f[2] * f[2]
    gain = jnp.maximum(vf, 0.0) / jnp.maximum(ff, 1.0)
    nv = [gain * f[c] + TIME_STEP * f[c] for c in range(3)]
    moved = [s_ref[image, c, here] + TIME_STEP * nv[c] for c in range(3)]
    length = jnp.sqrt(moved[0] * moved[0] + moved[1] * moved[1] + moved[2] * moved[2])
    for c in range(3):
        nv_ref[0, c] = nv[c]
        ns_ref[0, c] = moved[c] / length


def per_device(spins, velocity, upwind, climber, coupling):
    count, _, nx, ny, nz = spins.shape
    total = count * lax.axis_size("img")
    cells = nx * ny * nz * lax.axis_size("gx") * lax.axis_size("gy")
    root_cells = float(cells) ** 0.5
    indices = lax.axis_index("img") * count + jnp.arange(count, dtype=jnp.int32)
    ahead = from_behind(spins[:1], "img", -1)
    behind = from_behind(spins[-1:], "img", 1)
    field = lattice_field(spins, coupling)
    perp_field = field - cell_dot(field, spins) * spins
    after = jnp.concatenate([spins[1:], ahead], 0)
    before = jnp.concatenate([behind, spins[:-1]], 0)

    rows = ROWS if nx % ROWS == 0 else nx
    grid = (count, nx // rows)
    block = pl.BlockSpec((1, 3, rows, ny, nz), lambda i, j: (i, 0, j, 0, 0))
    small = pl.BlockSpec((1, 8, 128), lambda i, j: (i, 0, 0))
    smem = pl.BlockSpec(memory_space=pltpu.SMEM)
    whole = pl.BlockSpec(memory_space=pltpu.VMEM)
    params = pltpu.CompilerParams(
        dimension_semantics=("arbitrary", "arbitrary"), vmem_limit_bytes=VMEM_LIMIT
    )
    big = jax.ShapeDtypeStruct(spins.shape, jnp.float32)
    nbytes = spins.size * 4
    tangent_perp, sums = pl.pallas_call(
        functools.partial(tangent_kernel, rows),
        grid=grid,
        in_specs=[smem, whole, block, block, whole],
        out_specs=[whole, small],
        out_shape=[big, jax.ShapeDtypeStruct((count, 8, 128), jnp.float32)],
        scratch_shapes=[pltpu.VMEM((4, 8, nz), jnp.float32)],
        compiler_params=params,
        cost_estimate=pl.CostEstimate(flops=40 * spins.size, bytes_accessed=5 * nbytes, transcendentals=0),
    )(upwind, spins, after, before, perp_field)

    sums = group_sum(sums, ("gy", "gx"))
    climbing = indices == climber[0]
    ending = (indices == 0) | (indices == total - 1)
    flags = jnp.stack([climbing, ending], 0).astype(jnp.int32)
    new_spins, new_velocity, spacing = pl.pallas_call(
        functools.partial(update_kernel, root_cells, rows),
        grid=grid,
        in_specs=[smem, small, whole, whole, whole, whole],
        out_specs=[block, block, pl.BlockSpec((1, 1, 2), lambda i, j: (i, 0, 0))],
        out_shape=[big, big, jax.ShapeDtypeStruct((count, 1, 2), jnp.float32)],
        compiler_params=params,
        cost_estimate=pl.CostEstimate(flops=45 * spins.size, bytes_accessed=6 * nbytes, transcendentals=spins.size // 3),
    )(flags, sums, spins, velocity, perp_field, tangent_perp)
    return new_spins, new_velocity, spacing.reshape(count, 2)


def solution(mesh):
    return jax.shard_map(
        per_device,
        mesh=mesh,
        in_specs=(
            P("img", None, "gx", "gy", None),
            P("img", None, "gx", "gy", None),
            P("img"),
            P(),
            P(),
        ),
        out_specs=(
            P("img", None, "gx", "gy", None),
            P("img", None, "gx", "gy", None),
            P("img", None),
        ),
        check_vma=False,
    )
```

```python
import functools

import jax
import jax.numpy as jnp
from jax import lax
from jax.experimental import pallas as pl
from jax.experimental.pallas import tpu as pltpu
from jax.sharding import PartitionSpec as P

TIME_STEP = 0.1
SPRING = 2.0
EPSILON = 1e-06
ROWS = 4
VMEM_LIMIT = 8 * 1024 * 1024


def extended(block, sides, width):
    for axis, dim in sides:
        count = lax.axis_size(axis)
        forward = [(i, i + 1) for i in range(count - 1)]
        forward.append((count - 1, 0))
        backward = [(target, source) for source, target in forward]
        low = lax.ppermute(
            lax.slice_in_dim(block, block.shape[dim] - width, None, axis=dim), axis, forward
        )
        high = lax.ppermute(lax.slice_in_dim(block, 0, width, axis=dim), axis, backward)
        block = jnp.concatenate([low, block, high], axis=dim)
    return block


def from_behind(value, axis, by):
    size = lax.axis_size(axis)
    pairs = [(i, i + by) for i in range(size) if 0 <= i + by < size]
    return lax.ppermute(value, axis, pairs)


def add_kernel(a_ref, b_ref, o_ref):
    o_ref[...] = a_ref[...] + b_ref[...]


def small_add(a, b):
    whole = pl.BlockSpec(memory_space=pltpu.VMEM)
    return pl.pallas_call(
        add_kernel,
        in_specs=[whole, whole],
        out_specs=whole,
        out_shape=jax.ShapeDtypeStruct(a.shape, a.dtype),
        compiler_params=pltpu.CompilerParams(vmem_limit_bytes=1024 * 1024),
    )(a, b)


def group_sum(value, axes):
    for axis in axes:
        size = lax.axis_size(axis)
        if size & (size - 1):
            value = lax.psum(value, axis)
            continue
        step = 1
        while step < size:
            pairs = [(i, i ^ step) for i in range(size)]
            value = small_add(value, lax.ppermute(value, axis, pairs))
            step *= 2
    return value


def cell_dot(left, right):
    return jnp.sum(left * right, axis=1, keepdims=True)


def lattice_field(state, coupling):
    padded = extended(state, (("gx", 2), ("gy", 3)), 1)
    plus_x = padded[:, :, 2:, 1:-1]
    minus_x = padded[:, :, :-2, 1:-1]
    plus_y = padded[:, :, 1:-1, 2:]
    minus_y = padded[:, :, 1:-1, :-2]
    zpadded = jnp.pad(state, ((0, 0), (0, 0), (0, 0), (0, 0), (1, 1)))
    plus_z = zpadded[..., 2:]
    minus_z = zpadded[..., :-2]
    diff_x = plus_x - minus_x
    diff_y = plus_y - minus_y
    diff_z = plus_z - minus_z
    twist = jnp.stack(
        [diff_y[:, 2] - diff_z[:, 1], diff_z[:, 0] - diff_x[:, 2], diff_x[:, 1] - diff_y[:, 0]], 1
    )
    neighbours = plus_x + minus_x + plus_y + minus_y + plus_z + minus_z
    lift = jnp.array([0.0, 0.0, 1.0], jnp.float32).reshape(1, 3, 1, 1, 1)
    return coupling[0] * neighbours + coupling[1] * twist + coupling[2] * lift


def fold(x):
    return jnp.sum(x.reshape(-1, 8, x.shape[-1]), axis=0)


def tangent_kernel(rows, up_ref, s_ref, nx_ref, pv_ref, pf_ref, v_ref, tp_ref, sums_ref, acc_ref):
    image = pl.program_id(0)
    step = pl.program_id(1)
    here = pl.ds(pl.multiple_of(step * rows, rows), rows)

    @pl.when(step == 0)
    def _():
        acc_ref[...] = jnp.zeros_like(acc_ref)

    up = up_ref[pl.program_id(0)]
    ahead = jnp.where(up >= 0, 1.0, 0.0).astype(jnp.float32)
    behind = jnp.where(up <= 0, 1.0, 0.0).astype(jnp.float32)
    s = [s_ref[image, c, here] for c in range(3)]
    fwd = [nx_ref[0, c] - s[c] for c in range(3)]
    bwd = [s[c] - pv_ref[0, c] for c in range(3)]
    raw = [ahead * fwd[c] + behind * bwd[c] for c in range(3)]
    d = raw[0] * s[0] + raw[1] * s[1] + raw[2] * s[2]
    tp = [raw[c] - d * s[c] for c in range(3)]
    for c in range(3):
        tp_ref[image, c, here] = tp[c]
    pf = [pf_ref[image, c, here] for c in range(3)]
    acc_ref[0] += fold(tp[0] * tp[0] + tp[1] * tp[1] + tp[2] * tp[2])
    acc_ref[1] += fold(pf[0] * tp[0] + pf[1] * tp[1] + pf[2] * tp[2])
    acc_ref[2] += fold(fwd[0] * fwd[0] + fwd[1] * fwd[1] + fwd[2] * fwd[2])
    acc_ref[3] += fold(bwd[0] * bwd[0] + bwd[1] * bwd[1] + bwd[2] * bwd[2])

    @pl.when(step == pl.num_programs(1) - 1)
    def _():
        lane = lax.broadcasted_iota(jnp.int32, (8, 128), 1)
        row = lax.broadcasted_iota(jnp.int32, (8, 128), 0)
        out = jnp.zeros((8, 128), jnp.float32)
        for k in range(4):
            total = jnp.sum(acc_ref[k], keepdims=True)
            out = jnp.where((row == 0) & (lane == k), total, out)
        sums_ref[0] = out


def update_kernel(root_cells, rows, last, climber_ref, sums_ref, s_ref, v_ref, pf_ref, tp_ref, ns_ref, nv_ref, sp_ref):
    image = pl.program_id(0)
    here = pl.ds(pl.multiple_of(pl.program_id(1) * rows, rows), rows)
    tot = sums_ref[0]
    lane = lax.broadcasted_iota(jnp.int32, (8, 128), 1)
    row = lax.broadcasted_iota(jnp.int32, (8, 128), 0)

    def pick(k):
        return jnp.sum(jnp.where((row == 0) & (lane == k), tot, 0.0), keepdims=True)

    norm_t, along_t, next_sq, prev_sq = (pick(k) for k in range(4))
    scale = 1.0 / jnp.sqrt(norm_t + EPSILON)
    along = along_t * scale
    dist_next = jnp.sqrt(next_sq + EPSILON)
    dist_prev = jnp.sqrt(prev_sq + EPSILON)
    index = lax.axis_index("img") * pl.num_programs(0) + image
    climbing = jnp.full((1, 1), index) == climber_ref[0]
    ending = (jnp.full((1, 1), index) == 0) | (jnp.full((1, 1), index) == last)
    weight = jnp.where(climbing, 2.0 * along, along - SPRING * (dist_next - dist_prev))
    coef = jnp.where(ending, 0.0, weight * scale)
    keep = jnp.where(ending, 0.0, 1.0)

    @pl.when(pl.program_id(1) == 0)
    def _():
        pair = lax.broadcasted_iota(jnp.int32, (1, 2), 1)
        sp_ref[0] = jnp.where(pair == 0, dist_next, dist_prev) / root_cells

    f = [keep * pf_ref[image, c, here] - coef * tp_ref[image, c, here] for c in range(3)]
    v = [v_ref[image, c, here] for c in range(3)]
    vf = v[0] * f[0] + v[1] * f[1] + v[2] * f[2]
    ff = f[0] * f[0] + f[1] * f[1] + f[2] * f[2]
    gain = jnp.maximum(vf, 0.0) / jnp.maximum(ff, 1.0)
    nv = [gain * f[c] + TIME_STEP * f[c] for c in range(3)]
    moved = [s_ref[image, c, here] + TIME_STEP * nv[c] for c in range(3)]
    length = jnp.sqrt(moved[0] * moved[0] + moved[1] * moved[1] + moved[2] * moved[2])
    for c in range(3):
        nv_ref[0, c] = nv[c]
        ns_ref[0, c] = moved[c] / length


def per_device(spins, velocity, upwind, climber, coupling):
    count, _, nx, ny, nz = spins.shape
    total = count * lax.axis_size("img")
    cells = nx * ny * nz * lax.axis_size("gx") * lax.axis_size("gy")
    root_cells = float(cells) ** 0.5
    indices = lax.axis_index("img") * count + jnp.arange(count, dtype=jnp.int32)
    ahead = from_behind(spins[:1], "img", -1)
    behind = from_behind(spins[-1:], "img", 1)
    field = lattice_field(spins, coupling)
    perp_field = field - cell_dot(field, spins) * spins
    after = jnp.concatenate([spins[1:], ahead], 0)
    before = jnp.concatenate([behind, spins[:-1]], 0)

    rows = ROWS if nx % ROWS == 0 else nx
    grid = (count, nx // rows)
    block = pl.BlockSpec((1, 3, rows, ny, nz), lambda i, j: (i, 0, j, 0, 0))
    small = pl.BlockSpec((1, 8, 128), lambda i, j: (i, 0, 0))
    smem = pl.BlockSpec(memory_space=pltpu.SMEM)
    whole = pl.BlockSpec(memory_space=pltpu.VMEM)
    params = pltpu.CompilerParams(
        dimension_semantics=("arbitrary", "arbitrary"), vmem_limit_bytes=VMEM_LIMIT
    )
    big = jax.ShapeDtypeStruct(spins.shape, jnp.float32)
    nbytes = spins.size * 4
    tangent_perp, sums = pl.pallas_call(
        functools.partial(tangent_kernel, rows),
        grid=grid,
        in_specs=[smem, whole, block, block, whole, whole],
        out_specs=[whole, small],
        out_shape=[big, jax.ShapeDtypeStruct((count, 8, 128), jnp.float32)],
        scratch_shapes=[pltpu.VMEM((4, 8, nz), jnp.float32)],
        compiler_params=params,
        cost_estimate=pl.CostEstimate(flops=40 * spins.size, bytes_accessed=5 * nbytes, transcendentals=0),
    )(upwind, spins, after, before, perp_field, velocity)

    sums = group_sum(sums, ("gy", "gx"))
    new_spins, new_velocity, spacing = pl.pallas_call(
        functools.partial(update_kernel, root_cells, rows, total - 1),
        grid=grid,
        in_specs=[smem, small, whole, whole, whole, whole],
        out_specs=[block, block, pl.BlockSpec((1, 1, 2), lambda i, j: (i, 0, 0))],
        out_shape=[big, big, jax.ShapeDtypeStruct((count, 1, 2), jnp.float32)],
        compiler_params=params,
        cost_estimate=pl.CostEstimate(flops=45 * spins.size, bytes_accessed=6 * nbytes, transcendentals=spins.size // 3),
    )(climber, sums, spins, velocity, perp_field, tangent_perp)
    return new_spins, new_velocity, spacing.reshape(count, 2)


def solution(mesh):
    return jax.shard_map(
        per_device,
        mesh=mesh,
        in_specs=(
            P("img", None, "gx", "gy", None),
            P("img", None, "gx", "gy", None),
            P("img"),
            P(),
            P(),
        ),
        out_specs=(
            P("img", None, "gx", "gy", None),
            P("img", None, "gx", "gy", None),
            P("img", None),
        ),
        check_vma=False,
    )
```

```python
import functools

import jax
import jax.numpy as jnp
from jax import lax
from jax.experimental import pallas as pl
from jax.experimental.pallas import tpu as pltpu
from jax.sharding import PartitionSpec as P

TIME_STEP = 0.1
SPRING = 2.0
EPSILON = 1e-06
ROWS = 4
VMEM_LIMIT = 8 * 1024 * 1024


def extended(block, sides, width):
    for axis, dim in sides:
        count = lax.axis_size(axis)
        forward = [(i, i + 1) for i in range(count - 1)]
        forward.append((count - 1, 0))
        backward = [(target, source) for source, target in forward]
        low = lax.ppermute(
            lax.slice_in_dim(block, block.shape[dim] - width, None, axis=dim), axis, forward
        )
        high = lax.ppermute(lax.slice_in_dim(block, 0, width, axis=dim), axis, backward)
        block = jnp.concatenate([low, block, high], axis=dim)
    return block


def from_behind(value, axis, by):
    size = lax.axis_size(axis)
    pairs = [(i, i + by) for i in range(size) if 0 <= i + by < size]
    return lax.ppermute(value, axis, pairs)


def add_kernel(a_ref, b_ref, o_ref):
    o_ref[...] = a_ref[...] + b_ref[...]


def small_add(a, b):
    whole = pl.BlockSpec(memory_space=pltpu.VMEM)
    return pl.pallas_call(
        add_kernel,
        in_specs=[whole, whole],
        out_specs=whole,
        out_shape=jax.ShapeDtypeStruct(a.shape, a.dtype),
        compiler_params=pltpu.CompilerParams(vmem_limit_bytes=1024 * 1024),
    )(a, b)


def group_sum(value, axes):
    for axis in axes:
        size = lax.axis_size(axis)
        if size & (size - 1):
            value = lax.psum(value, axis)
            continue
        step = 1
        while step < size:
            pairs = [(i, i ^ step) for i in range(size)]
            value = small_add(value, lax.ppermute(value, axis, pairs))
            step *= 2
    return value


def cell_dot(left, right):
    return jnp.sum(left * right, axis=1, keepdims=True)


def lattice_field(state, coupling):
    padded = extended(state, (("gx", 2), ("gy", 3)), 1)
    plus_x = padded[:, :, 2:, 1:-1]
    minus_x = padded[:, :, :-2, 1:-1]
    plus_y = padded[:, :, 1:-1, 2:]
    minus_y = padded[:, :, 1:-1, :-2]
    zpadded = jnp.pad(state, ((0, 0), (0, 0), (0, 0), (0, 0), (1, 1)))
    plus_z = zpadded[..., 2:]
    minus_z = zpadded[..., :-2]
    diff_x = plus_x - minus_x
    diff_y = plus_y - minus_y
    diff_z = plus_z - minus_z
    twist = jnp.stack(
        [diff_y[:, 2] - diff_z[:, 1], diff_z[:, 0] - diff_x[:, 2], diff_x[:, 1] - diff_y[:, 0]], 1
    )
    neighbours = plus_x + minus_x + plus_y + minus_y + plus_z + minus_z
    lift = jnp.array([0.0, 0.0, 1.0], jnp.float32).reshape(1, 3, 1, 1, 1)
    return coupling[0] * neighbours + coupling[1] * twist + coupling[2] * lift


def fold(x):
    return jnp.sum(x.reshape(-1, 8, x.shape[-1]), axis=0)


def tangent_kernel(rows, up_ref, s_ref, nx_ref, pv_ref, pf_ref, v_ref, tp_ref, sums_ref, acc_ref):
    image = pl.program_id(0)
    step = pl.program_id(1)
    here = pl.ds(pl.multiple_of(step * rows, rows), rows)

    @pl.when(step == 0)
    def _():
        acc_ref[...] = jnp.zeros_like(acc_ref)

    up = up_ref[pl.program_id(0)]
    ahead = jnp.where(up >= 0, 1.0, 0.0).astype(jnp.float32)
    behind = jnp.where(up <= 0, 1.0, 0.0).astype(jnp.float32)
    s = [s_ref[image, c, here] for c in range(3)]
    fwd = [nx_ref[0, c] - s[c] for c in range(3)]
    bwd = [s[c] - pv_ref[0, c] for c in range(3)]
    raw = [ahead * fwd[c] + behind * bwd[c] for c in range(3)]
    d = raw[0] * s[0] + raw[1] * s[1] + raw[2] * s[2]
    tp = [raw[c] - d * s[c] for c in range(3)]
    for c in range(3):
        tp_ref[image, c, here] = tp[c]
    pf = [pf_ref[image, c, here] for c in range(3)]
    acc_ref[0] += fold(tp[0] * tp[0] + tp[1] * tp[1] + tp[2] * tp[2])
    acc_ref[1] += fold(pf[0] * tp[0] + pf[1] * tp[1] + pf[2] * tp[2])
    acc_ref[2] += fold(fwd[0] * fwd[0] + fwd[1] * fwd[1] + fwd[2] * fwd[2])
    acc_ref[3] += fold(bwd[0] * bwd[0] + bwd[1] * bwd[1] + bwd[2] * bwd[2])

    @pl.when(step == pl.num_programs(1) - 1)
    def _():
        lane = lax.broadcasted_iota(jnp.int32, (8, 128), 1)
        row = lax.broadcasted_iota(jnp.int32, (8, 128), 0)
        out = jnp.zeros((8, 128), jnp.float32)
        for k in range(4):
            total = jnp.sum(acc_ref[k], keepdims=True)
            out = jnp.where((row == 0) & (lane == k), total, out)
        sums_ref[0] = out


def update_kernel(root_cells, rows, last, climber_ref, sums_ref, s_ref, v_ref, pf_ref, tp_ref, ns_ref, nv_ref, sp_ref):
    image = pl.program_id(0)
    here = pl.ds(pl.multiple_of(pl.program_id(1) * rows, rows), rows)
    tot = sums_ref[0]
    lane = lax.broadcasted_iota(jnp.int32, (8, 128), 1)
    row = lax.broadcasted_iota(jnp.int32, (8, 128), 0)

    def pick(k):
        return jnp.sum(jnp.where((row == 0) & (lane == k), tot, 0.0), keepdims=True)

    norm_t, along_t, next_sq, prev_sq = (pick(k) for k in range(4))
    scale = 1.0 / jnp.sqrt(norm_t + EPSILON)
    along = along_t * scale
    dist_next = jnp.sqrt(next_sq + EPSILON)
    dist_prev = jnp.sqrt(prev_sq + EPSILON)
    index = lax.axis_index("img") * pl.num_programs(0) + image
    climbing = jnp.full((1, 1), index) == climber_ref[0]
    ending = (jnp.full((1, 1), index) == 0) | (jnp.full((1, 1), index) == last)
    weight = jnp.where(climbing, 2.0 * along, along - SPRING * (dist_next - dist_prev))
    coef = jnp.where(ending, 0.0, weight * scale)
    keep = jnp.where(ending, 0.0, 1.0)

    @pl.when(pl.program_id(1) == 0)
    def _():
        pair = lax.broadcasted_iota(jnp.int32, (1, 2), 1)
        sp_ref[0] = jnp.where(pair == 0, dist_next, dist_prev) / root_cells

    f = [keep * pf_ref[image, c, here] - coef * tp_ref[image, c, here] for c in range(3)]
    v = [v_ref[image, c, here] for c in range(3)]
    vf = v[0] * f[0] + v[1] * f[1] + v[2] * f[2]
    ff = f[0] * f[0] + f[1] * f[1] + f[2] * f[2]
    gain = jnp.maximum(vf, 0.0) / jnp.maximum(ff, 1.0)
    nv = [gain * f[c] + TIME_STEP * f[c] for c in range(3)]
    moved = [s_ref[image, c, here] + TIME_STEP * nv[c] for c in range(3)]
    inverse = lax.rsqrt(moved[0] * moved[0] + moved[1] * moved[1] + moved[2] * moved[2])
    for c in range(3):
        nv_ref[0, c] = nv[c]
        ns_ref[0, c] = moved[c] * inverse


def per_device(spins, velocity, upwind, climber, coupling):
    count, _, nx, ny, nz = spins.shape
    total = count * lax.axis_size("img")
    cells = nx * ny * nz * lax.axis_size("gx") * lax.axis_size("gy")
    root_cells = float(cells) ** 0.5
    indices = lax.axis_index("img") * count + jnp.arange(count, dtype=jnp.int32)
    ahead = from_behind(spins[:1], "img", -1)
    behind = from_behind(spins[-1:], "img", 1)
    field = lattice_field(spins, coupling)
    perp_field = field - cell_dot(field, spins) * spins
    after = jnp.concatenate([spins[1:], ahead], 0)
    before = jnp.concatenate([behind, spins[:-1]], 0)

    rows = ROWS if nx % ROWS == 0 else nx
    grid = (count, nx // rows)
    block = pl.BlockSpec((1, 3, rows, ny, nz), lambda i, j: (i, 0, j, 0, 0))
    small = pl.BlockSpec((1, 8, 128), lambda i, j: (i, 0, 0))
    smem = pl.BlockSpec(memory_space=pltpu.SMEM)
    whole = pl.BlockSpec(memory_space=pltpu.VMEM)
    params = pltpu.CompilerParams(
        dimension_semantics=("arbitrary", "arbitrary"), vmem_limit_bytes=VMEM_LIMIT
    )
    big = jax.ShapeDtypeStruct(spins.shape, jnp.float32)
    nbytes = spins.size * 4
    tangent_perp, sums = pl.pallas_call(
        functools.partial(tangent_kernel, rows),
        grid=grid,
        in_specs=[smem, whole, block, block, whole, whole],
        out_specs=[whole, small],
        out_shape=[big, jax.ShapeDtypeStruct((count, 8, 128), jnp.float32)],
        scratch_shapes=[pltpu.VMEM((4, 8, nz), jnp.float32)],
        compiler_params=params,
        cost_estimate=pl.CostEstimate(flops=40 * spins.size, bytes_accessed=5 * nbytes, transcendentals=0),
    )(upwind, spins, after, before, perp_field, velocity)

    sums = group_sum(sums, ("gy", "gx"))
    new_spins, new_velocity, spacing = pl.pallas_call(
        functools.partial(update_kernel, root_cells, rows, total - 1),
        grid=grid,
        in_specs=[smem, small, whole, whole, whole, whole],
        out_specs=[block, block, pl.BlockSpec((1, 1, 2), lambda i, j: (i, 0, 0))],
        out_shape=[big, big, jax.ShapeDtypeStruct((count, 1, 2), jnp.float32)],
        compiler_params=params,
        cost_estimate=pl.CostEstimate(flops=45 * spins.size, bytes_accessed=6 * nbytes, transcendentals=spins.size // 3),
    )(climber, sums, spins, velocity, perp_field, tangent_perp)
    return new_spins, new_velocity, spacing.reshape(count, 2)


def solution(mesh):
    return jax.shard_map(
        per_device,
        mesh=mesh,
        in_specs=(
            P("img", None, "gx", "gy", None),
            P("img", None, "gx", "gy", None),
            P("img"),
            P(),
            P(),
        ),
        out_specs=(
            P("img", None, "gx", "gy", None),
            P("img", None, "gx", "gy", None),
            P("img", None),
        ),
        check_vma=False,
    )
```

```python
import functools

import jax
import jax.numpy as jnp
from jax import lax
from jax.experimental import pallas as pl
from jax.experimental.pallas import tpu as pltpu
from jax.sharding import PartitionSpec as P

TIME_STEP = 0.1
SPRING = 2.0
EPSILON = 1e-06
ROWS = 8
ROWS_A = 8
VMEM_LIMIT = 8 * 1024 * 1024


def extended(block, sides, width):
    for axis, dim in sides:
        count = lax.axis_size(axis)
        forward = [(i, i + 1) for i in range(count - 1)]
        forward.append((count - 1, 0))
        backward = [(target, source) for source, target in forward]
        low = lax.ppermute(
            lax.slice_in_dim(block, block.shape[dim] - width, None, axis=dim), axis, forward
        )
        high = lax.ppermute(lax.slice_in_dim(block, 0, width, axis=dim), axis, backward)
        block = jnp.concatenate([low, block, high], axis=dim)
    return block


def from_behind(value, axis, by):
    size = lax.axis_size(axis)
    pairs = [(i, i + by) for i in range(size) if 0 <= i + by < size]
    return lax.ppermute(value, axis, pairs)


def add_kernel(a_ref, b_ref, o_ref):
    o_ref[...] = a_ref[...] + b_ref[...]


def small_add(a, b):
    whole = pl.BlockSpec(memory_space=pltpu.VMEM)
    return pl.pallas_call(
        add_kernel,
        in_specs=[whole, whole],
        out_specs=whole,
        out_shape=jax.ShapeDtypeStruct(a.shape, a.dtype),
        compiler_params=pltpu.CompilerParams(vmem_limit_bytes=1024 * 1024),
    )(a, b)


def group_sum(value, axes):
    for axis in axes:
        size = lax.axis_size(axis)
        if size & (size - 1):
            value = lax.psum(value, axis)
            continue
        step = 1
        while step < size:
            pairs = [(i, i ^ step) for i in range(size)]
            value = small_add(value, lax.ppermute(value, axis, pairs))
            step *= 2
    return value


def cell_dot(left, right):
    return jnp.sum(left * right, axis=1, keepdims=True)


def lattice_field(state, coupling):
    padded = extended(state, (("gx", 2), ("gy", 3)), 1)
    plus_x = padded[:, :, 2:, 1:-1]
    minus_x = padded[:, :, :-2, 1:-1]
    plus_y = padded[:, :, 1:-1, 2:]
    minus_y = padded[:, :, 1:-1, :-2]
    zpadded = jnp.pad(state, ((0, 0), (0, 0), (0, 0), (0, 0), (1, 1)))
    plus_z = zpadded[..., 2:]
    minus_z = zpadded[..., :-2]
    diff_x = plus_x - minus_x
    diff_y = plus_y - minus_y
    diff_z = plus_z - minus_z
    twist = jnp.stack(
        [diff_y[:, 2] - diff_z[:, 1], diff_z[:, 0] - diff_x[:, 2], diff_x[:, 1] - diff_y[:, 0]], 1
    )
    neighbours = plus_x + minus_x + plus_y + minus_y + plus_z + minus_z
    lift = jnp.array([0.0, 0.0, 1.0], jnp.float32).reshape(1, 3, 1, 1, 1)
    return coupling[0] * neighbours + coupling[1] * twist + coupling[2] * lift


def fold(x):
    return jnp.sum(x.reshape(-1, 8, x.shape[-1]), axis=0)


def tangent_kernel(rows, up_ref, s_ref, nx_ref, pv_ref, pf_ref, v_ref, tp_ref, sums_ref, acc_ref):
    image = pl.program_id(0)
    step = pl.program_id(1)
    here = pl.ds(pl.multiple_of(step * rows, rows), rows)

    @pl.when(step == 0)
    def _():
        acc_ref[...] = jnp.zeros_like(acc_ref)

    up = up_ref[pl.program_id(0)]
    ahead = jnp.where(up >= 0, 1.0, 0.0).astype(jnp.float32)
    behind = jnp.where(up <= 0, 1.0, 0.0).astype(jnp.float32)
    s = [s_ref[image, c, here] for c in range(3)]
    fwd = [nx_ref[image, c, here] - s[c] for c in range(3)]
    bwd = [s[c] - pv_ref[image, c, here] for c in range(3)]
    raw = [ahead * fwd[c] + behind * bwd[c] for c in range(3)]
    d = raw[0] * s[0] + raw[1] * s[1] + raw[2] * s[2]
    tp = [raw[c] - d * s[c] for c in range(3)]
    for c in range(3):
        tp_ref[image, c, here] = tp[c]
    pf = [pf_ref[image, c, here] for c in range(3)]
    acc_ref[0] += fold(tp[0] * tp[0] + tp[1] * tp[1] + tp[2] * tp[2])
    acc_ref[1] += fold(pf[0] * tp[0] + pf[1] * tp[1] + pf[2] * tp[2])
    acc_ref[2] += fold(fwd[0] * fwd[0] + fwd[1] * fwd[1] + fwd[2] * fwd[2])
    acc_ref[3] += fold(bwd[0] * bwd[0] + bwd[1] * bwd[1] + bwd[2] * bwd[2])

    @pl.when(step == pl.num_programs(1) - 1)
    def _():
        lane = lax.broadcasted_iota(jnp.int32, (8, 128), 1)
        row = lax.broadcasted_iota(jnp.int32, (8, 128), 0)
        out = jnp.zeros((8, 128), jnp.float32)
        for k in range(4):
            total = jnp.sum(acc_ref[k], keepdims=True)
            out = jnp.where((row == 0) & (lane == k), total, out)
        sums_ref[0] = out


def update_kernel(root_cells, rows, last, climber_ref, sums_ref, s_ref, v_ref, pf_ref, tp_ref, ns_ref, nv_ref, sp_ref):
    image = pl.program_id(0)
    here = pl.ds(pl.multiple_of(pl.program_id(1) * rows, rows), rows)
    tot = sums_ref[0]
    lane = lax.broadcasted_iota(jnp.int32, (8, 128), 1)
    row = lax.broadcasted_iota(jnp.int32, (8, 128), 0)

    def pick(k):
        return jnp.sum(jnp.where((row == 0) & (lane == k), tot, 0.0), keepdims=True)

    norm_t, along_t, next_sq, prev_sq = (pick(k) for k in range(4))
    scale = 1.0 / jnp.sqrt(norm_t + EPSILON)
    along = along_t * scale
    dist_next = jnp.sqrt(next_sq + EPSILON)
    dist_prev = jnp.sqrt(prev_sq + EPSILON)
    index = lax.axis_index("img") * pl.num_programs(0) + image
    climbing = jnp.full((1, 1), index) == climber_ref[0]
    ending = (jnp.full((1, 1), index) == 0) | (jnp.full((1, 1), index) == last)
    weight = jnp.where(climbing, 2.0 * along, along - SPRING * (dist_next - dist_prev))
    coef = jnp.where(ending, 0.0, weight * scale)
    keep = jnp.where(ending, 0.0, 1.0)

    @pl.when(pl.program_id(1) == 0)
    def _():
        pair = lax.broadcasted_iota(jnp.int32, (1, 2), 1)
        sp_ref[0] = jnp.where(pair == 0, dist_next, dist_prev) / root_cells

    f = [keep * pf_ref[image, c, here] - coef * tp_ref[image, c, here] for c in range(3)]
    v = [v_ref[image, c, here] for c in range(3)]
    vf = v[0] * f[0] + v[1] * f[1] + v[2] * f[2]
    ff = f[0] * f[0] + f[1] * f[1] + f[2] * f[2]
    gain = jnp.maximum(vf, 0.0) / jnp.maximum(ff, 1.0)
    nv = [gain * f[c] + TIME_STEP * f[c] for c in range(3)]
    moved = [s_ref[image, c, here] + TIME_STEP * nv[c] for c in range(3)]
    inverse = lax.rsqrt(moved[0] * moved[0] + moved[1] * moved[1] + moved[2] * moved[2])
    for c in range(3):
        nv_ref[0, c] = nv[c]
        ns_ref[0, c] = moved[c] * inverse


def per_device(spins, velocity, upwind, climber, coupling):
    count, _, nx, ny, nz = spins.shape
    total = count * lax.axis_size("img")
    cells = nx * ny * nz * lax.axis_size("gx") * lax.axis_size("gy")
    root_cells = float(cells) ** 0.5
    indices = lax.axis_index("img") * count + jnp.arange(count, dtype=jnp.int32)
    ahead = from_behind(spins[:1], "img", -1)
    behind = from_behind(spins[-1:], "img", 1)
    field = lattice_field(spins, coupling)
    perp_field = field - cell_dot(field, spins) * spins
    after = jnp.concatenate([spins[1:], ahead], 0)
    before = jnp.concatenate([behind, spins[:-1]], 0)

    rows = ROWS if nx % ROWS == 0 else nx
    grid = (count, nx // rows)
    block = pl.BlockSpec((1, 3, rows, ny, nz), lambda i, j: (i, 0, j, 0, 0))
    small = pl.BlockSpec((1, 8, 128), lambda i, j: (i, 0, 0))
    smem = pl.BlockSpec(memory_space=pltpu.SMEM)
    whole = pl.BlockSpec(memory_space=pltpu.VMEM)
    params = pltpu.CompilerParams(
        dimension_semantics=("arbitrary", "arbitrary"), vmem_limit_bytes=VMEM_LIMIT
    )
    big = jax.ShapeDtypeStruct(spins.shape, jnp.float32)
    nbytes = spins.size * 4
    rows_a = ROWS_A if nx % ROWS_A == 0 else nx
    tangent_perp, sums = pl.pallas_call(
        functools.partial(tangent_kernel, rows_a),
        grid=(count, nx // rows_a),
        in_specs=[smem, whole, whole, whole, whole, whole],
        out_specs=[whole, small],
        out_shape=[big, jax.ShapeDtypeStruct((count, 8, 128), jnp.float32)],
        scratch_shapes=[pltpu.VMEM((4, 8, nz), jnp.float32)],
        compiler_params=params,
        cost_estimate=pl.CostEstimate(flops=40 * spins.size, bytes_accessed=5 * nbytes, transcendentals=0),
    )(upwind, spins, after, before, perp_field, velocity)

    sums = group_sum(sums, ("gy", "gx"))
    new_spins, new_velocity, spacing = pl.pallas_call(
        functools.partial(update_kernel, root_cells, rows, total - 1),
        grid=grid,
        in_specs=[smem, small, whole, whole, whole, whole],
        out_specs=[block, block, pl.BlockSpec((1, 1, 2), lambda i, j: (i, 0, 0))],
        out_shape=[big, big, jax.ShapeDtypeStruct((count, 1, 2), jnp.float32)],
        compiler_params=params,
        cost_estimate=pl.CostEstimate(flops=45 * spins.size, bytes_accessed=6 * nbytes, transcendentals=spins.size // 3),
    )(climber, sums, spins, velocity, perp_field, tangent_perp)
    return new_spins, new_velocity, spacing.reshape(count, 2)


def solution(mesh):
    return jax.shard_map(
        per_device,
        mesh=mesh,
        in_specs=(
            P("img", None, "gx", "gy", None),
            P("img", None, "gx", "gy", None),
            P("img"),
            P(),
            P(),
        ),
        out_specs=(
            P("img", None, "gx", "gy", None),
            P("img", None, "gx", "gy", None),
            P("img", None),
        ),
        check_vma=False,
    )
```

```python
import functools

import jax
import jax.numpy as jnp
from jax import lax
from jax.experimental import pallas as pl
from jax.experimental.pallas import tpu as pltpu
from jax.sharding import PartitionSpec as P

TIME_STEP = 0.1
SPRING = 2.0
EPSILON = 1e-06
ROWS = 8
ROWS_A = 8
VMEM_LIMIT = 8 * 1024 * 1024


def extended(block, sides, width):
    for axis, dim in sides:
        count = lax.axis_size(axis)
        forward = [(i, i + 1) for i in range(count - 1)]
        forward.append((count - 1, 0))
        backward = [(target, source) for source, target in forward]
        low = lax.ppermute(
            lax.slice_in_dim(block, block.shape[dim] - width, None, axis=dim), axis, forward
        )
        high = lax.ppermute(lax.slice_in_dim(block, 0, width, axis=dim), axis, backward)
        block = jnp.concatenate([low, block, high], axis=dim)
    return block


def from_behind(value, axis, by):
    size = lax.axis_size(axis)
    pairs = [(i, i + by) for i in range(size) if 0 <= i + by < size]
    return lax.ppermute(value, axis, pairs)


def add_kernel(a_ref, b_ref, o_ref):
    o_ref[...] = a_ref[...] + b_ref[...]


def small_add(a, b):
    whole = pl.BlockSpec(memory_space=pltpu.VMEM)
    return pl.pallas_call(
        add_kernel,
        in_specs=[whole, whole],
        out_specs=whole,
        out_shape=jax.ShapeDtypeStruct(a.shape, a.dtype),
        compiler_params=pltpu.CompilerParams(vmem_limit_bytes=1024 * 1024),
    )(a, b)


def group_sum(value, axes):
    for axis in axes:
        size = lax.axis_size(axis)
        if size & (size - 1):
            value = lax.psum(value, axis)
            continue
        step = 1
        while step < size:
            pairs = [(i, i ^ step) for i in range(size)]
            value = small_add(value, lax.ppermute(value, axis, pairs))
            step *= 2
    return value


def cell_dot(left, right):
    return jnp.sum(left * right, axis=1, keepdims=True)


def lattice_field(state, coupling):
    padded = extended(state, (("gx", 2), ("gy", 3)), 1)
    plus_x = padded[:, :, 2:, 1:-1]
    minus_x = padded[:, :, :-2, 1:-1]
    plus_y = padded[:, :, 1:-1, 2:]
    minus_y = padded[:, :, 1:-1, :-2]
    zpadded = jnp.pad(state, ((0, 0), (0, 0), (0, 0), (0, 0), (1, 1)))
    plus_z = zpadded[..., 2:]
    minus_z = zpadded[..., :-2]
    diff_x = plus_x - minus_x
    diff_y = plus_y - minus_y
    diff_z = plus_z - minus_z
    twist = jnp.stack(
        [diff_y[:, 2] - diff_z[:, 1], diff_z[:, 0] - diff_x[:, 2], diff_x[:, 1] - diff_y[:, 0]], 1
    )
    neighbours = plus_x + minus_x + plus_y + minus_y + plus_z + minus_z
    lift = jnp.array([0.0, 0.0, 1.0], jnp.float32).reshape(1, 3, 1, 1, 1)
    return coupling[0] * neighbours + coupling[1] * twist + coupling[2] * lift


def fold(x):
    return jnp.sum(x.reshape(-1, 8, x.shape[-1]), axis=0)


def tangent_kernel(rows, up_ref, s_ref, first_ref, second_ref, pf_ref, v_ref, tp_ref, sums_ref, acc_ref):
    image = pl.program_id(0)
    step = pl.program_id(1)
    here = pl.ds(pl.multiple_of(step * rows, rows), rows)
    even = jnp.full((1, 1, 1), lax.axis_index("img") % 2) == 0

    @pl.when(step == 0)
    def _():
        acc_ref[...] = jnp.zeros_like(acc_ref)

    up = up_ref[pl.program_id(0)]
    ahead = jnp.where(up >= 0, 1.0, 0.0).astype(jnp.float32)
    behind = jnp.where(up <= 0, 1.0, 0.0).astype(jnp.float32)
    s = [s_ref[image, c, here] for c in range(3)]
    first = [first_ref[image, c, here] for c in range(3)]
    second = [second_ref[image, c, here] for c in range(3)]
    fwd = [jnp.where(even, first[c], second[c]) - s[c] for c in range(3)]
    bwd = [s[c] - jnp.where(even, second[c], first[c]) for c in range(3)]
    raw = [ahead * fwd[c] + behind * bwd[c] for c in range(3)]
    d = raw[0] * s[0] + raw[1] * s[1] + raw[2] * s[2]
    tp = [raw[c] - d * s[c] for c in range(3)]
    for c in range(3):
        tp_ref[image, c, here] = tp[c]
    pf = [pf_ref[image, c, here] for c in range(3)]
    acc_ref[0] += fold(tp[0] * tp[0] + tp[1] * tp[1] + tp[2] * tp[2])
    acc_ref[1] += fold(pf[0] * tp[0] + pf[1] * tp[1] + pf[2] * tp[2])
    acc_ref[2] += fold(fwd[0] * fwd[0] + fwd[1] * fwd[1] + fwd[2] * fwd[2])
    acc_ref[3] += fold(bwd[0] * bwd[0] + bwd[1] * bwd[1] + bwd[2] * bwd[2])

    @pl.when(step == pl.num_programs(1) - 1)
    def _():
        lane = lax.broadcasted_iota(jnp.int32, (8, 128), 1)
        row = lax.broadcasted_iota(jnp.int32, (8, 128), 0)
        out = jnp.zeros((8, 128), jnp.float32)
        for k in range(4):
            total = jnp.sum(acc_ref[k], keepdims=True)
            out = jnp.where((row == 0) & (lane == k), total, out)
        sums_ref[0] = out


def update_kernel(root_cells, rows, last, climber_ref, sums_ref, s_ref, v_ref, pf_ref, tp_ref, ns_ref, nv_ref, sp_ref):
    image = pl.program_id(0)
    here = pl.ds(pl.multiple_of(pl.program_id(1) * rows, rows), rows)
    tot = sums_ref[0]
    lane = lax.broadcasted_iota(jnp.int32, (8, 128), 1)
    row = lax.broadcasted_iota(jnp.int32, (8, 128), 0)

    def pick(k):
        return jnp.sum(jnp.where((row == 0) & (lane == k), tot, 0.0), keepdims=True)

    norm_t, along_t, next_sq, prev_sq = (pick(k) for k in range(4))
    scale = 1.0 / jnp.sqrt(norm_t + EPSILON)
    along = along_t * scale
    dist_next = jnp.sqrt(next_sq + EPSILON)
    dist_prev = jnp.sqrt(prev_sq + EPSILON)
    index = lax.axis_index("img") * pl.num_programs(0) + image
    climbing = jnp.full((1, 1), index) == climber_ref[0]
    ending = (jnp.full((1, 1), index) == 0) | (jnp.full((1, 1), index) == last)
    weight = jnp.where(climbing, 2.0 * along, along - SPRING * (dist_next - dist_prev))
    coef = jnp.where(ending, 0.0, weight * scale)
    keep = jnp.where(ending, 0.0, 1.0)

    @pl.when(pl.program_id(1) == 0)
    def _():
        pair = lax.broadcasted_iota(jnp.int32, (1, 2), 1)
        sp_ref[0] = jnp.where(pair == 0, dist_next, dist_prev) / root_cells

    f = [keep * pf_ref[image, c, here] - coef * tp_ref[image, c, here] for c in range(3)]
    v = [v_ref[image, c, here] for c in range(3)]
    vf = v[0] * f[0] + v[1] * f[1] + v[2] * f[2]
    ff = f[0] * f[0] + f[1] * f[1] + f[2] * f[2]
    gain = jnp.maximum(vf, 0.0) / jnp.maximum(ff, 1.0)
    nv = [gain * f[c] + TIME_STEP * f[c] for c in range(3)]
    moved = [s_ref[image, c, here] + TIME_STEP * nv[c] for c in range(3)]
    inverse = lax.rsqrt(moved[0] * moved[0] + moved[1] * moved[1] + moved[2] * moved[2])
    for c in range(3):
        nv_ref[0, c] = nv[c]
        ns_ref[0, c] = moved[c] * inverse


def per_device(spins, velocity, upwind, climber, coupling):
    count, _, nx, ny, nz = spins.shape
    total = count * lax.axis_size("img")
    cells = nx * ny * nz * lax.axis_size("gx") * lax.axis_size("gy")
    root_cells = float(cells) ** 0.5
    indices = lax.axis_index("img") * count + jnp.arange(count, dtype=jnp.int32)
    assert count == 1
    places = lax.axis_size("img")
    first = lax.ppermute(spins, "img", [(i, i ^ 1) for i in range(places) if i ^ 1 < places])
    second = lax.ppermute(
        spins, "img", [(i, i - 1 + 2 * (i % 2)) for i in range(1, places - 1)]
    )
    field = lattice_field(spins, coupling)
    perp_field = field - cell_dot(field, spins) * spins

    rows = ROWS if nx % ROWS == 0 else nx
    grid = (count, nx // rows)
    block = pl.BlockSpec((1, 3, rows, ny, nz), lambda i, j: (i, 0, j, 0, 0))
    small = pl.BlockSpec((1, 8, 128), lambda i, j: (i, 0, 0))
    smem = pl.BlockSpec(memory_space=pltpu.SMEM)
    whole = pl.BlockSpec(memory_space=pltpu.VMEM)
    params = pltpu.CompilerParams(
        dimension_semantics=("arbitrary", "arbitrary"), vmem_limit_bytes=VMEM_LIMIT
    )
    big = jax.ShapeDtypeStruct(spins.shape, jnp.float32)
    nbytes = spins.size * 4
    rows_a = ROWS_A if nx % ROWS_A == 0 else nx
    tangent_perp, sums = pl.pallas_call(
        functools.partial(tangent_kernel, rows_a),
        grid=(count, nx // rows_a),
        in_specs=[smem, whole, whole, whole, whole, whole],
        out_specs=[whole, small],
        out_shape=[big, jax.ShapeDtypeStruct((count, 8, 128), jnp.float32)],
        scratch_shapes=[pltpu.VMEM((4, 8, nz), jnp.float32)],
        compiler_params=params,
        cost_estimate=pl.CostEstimate(flops=40 * spins.size, bytes_accessed=5 * nbytes, transcendentals=0),
    )(upwind, spins, first, second, perp_field, velocity)

    sums = group_sum(sums, ("gy", "gx"))
    new_spins, new_velocity, spacing = pl.pallas_call(
        functools.partial(update_kernel, root_cells, rows, total - 1),
        grid=grid,
        in_specs=[smem, small, whole, whole, whole, whole],
        out_specs=[block, block, pl.BlockSpec((1, 1, 2), lambda i, j: (i, 0, 0))],
        out_shape=[big, big, jax.ShapeDtypeStruct((count, 1, 2), jnp.float32)],
        compiler_params=params,
        cost_estimate=pl.CostEstimate(flops=45 * spins.size, bytes_accessed=6 * nbytes, transcendentals=spins.size // 3),
    )(climber, sums, spins, velocity, perp_field, tangent_perp)
    return new_spins, new_velocity, spacing.reshape(count, 2)


def solution(mesh):
    return jax.shard_map(
        per_device,
        mesh=mesh,
        in_specs=(
            P("img", None, "gx", "gy", None),
            P("img", None, "gx", "gy", None),
            P("img"),
            P(),
            P(),
        ),
        out_specs=(
            P("img", None, "gx", "gy", None),
            P("img", None, "gx", "gy", None),
            P("img", None),
        ),
        check_vma=False,
    )
```

```python
import functools

import jax
import jax.numpy as jnp
from jax import lax
from jax.experimental import pallas as pl
from jax.experimental.pallas import tpu as pltpu
from jax.sharding import PartitionSpec as P

TIME_STEP = 0.1
SPRING = 2.0
EPSILON = 1e-06
ROWS = 16
ROWS_A = 8
VMEM_LIMIT = 16 * 1024 * 1024


def extended(block, sides, width):
    for axis, dim in sides:
        count = lax.axis_size(axis)
        forward = [(i, i + 1) for i in range(count - 1)]
        forward.append((count - 1, 0))
        backward = [(target, source) for source, target in forward]
        low = lax.ppermute(
            lax.slice_in_dim(block, block.shape[dim] - width, None, axis=dim), axis, forward
        )
        high = lax.ppermute(lax.slice_in_dim(block, 0, width, axis=dim), axis, backward)
        block = jnp.concatenate([low, block, high], axis=dim)
    return block


def from_behind(value, axis, by):
    size = lax.axis_size(axis)
    pairs = [(i, i + by) for i in range(size) if 0 <= i + by < size]
    return lax.ppermute(value, axis, pairs)


def add_kernel(a_ref, b_ref, o_ref):
    o_ref[...] = a_ref[...] + b_ref[...]


def small_add(a, b):
    whole = pl.BlockSpec(memory_space=pltpu.VMEM)
    return pl.pallas_call(
        add_kernel,
        in_specs=[whole, whole],
        out_specs=whole,
        out_shape=jax.ShapeDtypeStruct(a.shape, a.dtype),
        compiler_params=pltpu.CompilerParams(vmem_limit_bytes=1024 * 1024),
    )(a, b)


def group_sum(value, axes):
    for axis in axes:
        size = lax.axis_size(axis)
        if size & (size - 1):
            value = lax.psum(value, axis)
            continue
        step = 1
        while step < size:
            pairs = [(i, i ^ step) for i in range(size)]
            value = small_add(value, lax.ppermute(value, axis, pairs))
            step *= 2
    return value


def cell_dot(left, right):
    return jnp.sum(left * right, axis=1, keepdims=True)


def lattice_field(state, coupling):
    padded = extended(state, (("gx", 2), ("gy", 3)), 1)
    plus_x = padded[:, :, 2:, 1:-1]
    minus_x = padded[:, :, :-2, 1:-1]
    plus_y = padded[:, :, 1:-1, 2:]
    minus_y = padded[:, :, 1:-1, :-2]
    zpadded = jnp.pad(state, ((0, 0), (0, 0), (0, 0), (0, 0), (1, 1)))
    plus_z = zpadded[..., 2:]
    minus_z = zpadded[..., :-2]
    diff_x = plus_x - minus_x
    diff_y = plus_y - minus_y
    diff_z = plus_z - minus_z
    twist = jnp.stack(
        [diff_y[:, 2] - diff_z[:, 1], diff_z[:, 0] - diff_x[:, 2], diff_x[:, 1] - diff_y[:, 0]], 1
    )
    neighbours = plus_x + minus_x + plus_y + minus_y + plus_z + minus_z
    lift = jnp.array([0.0, 0.0, 1.0], jnp.float32).reshape(1, 3, 1, 1, 1)
    return coupling[0] * neighbours + coupling[1] * twist + coupling[2] * lift


def fold(x):
    return jnp.sum(x.reshape(-1, 8, x.shape[-1]), axis=0)


def tangent_kernel(rows, up_ref, s_ref, first_ref, second_ref, pf_ref, v_ref, tp_ref, sums_ref, acc_ref):
    image = pl.program_id(0)
    step = pl.program_id(1)
    here = pl.ds(pl.multiple_of(step * rows, rows), rows)
    even = lax.axis_index("img") % 2 == 0
    up = up_ref[image]

    @pl.when(step == 0)
    def _():
        acc_ref[...] = jnp.zeros_like(acc_ref)

    def body(nx_ref, pv_ref, mode):
        s = [s_ref[image, c, here] for c in range(3)]
        fwd = [nx_ref[image, c, here] - s[c] for c in range(3)]
        bwd = [s[c] - pv_ref[image, c, here] for c in range(3)]
        if mode > 0:
            raw = fwd
        elif mode < 0:
            raw = bwd
        else:
            raw = [fwd[c] + bwd[c] for c in range(3)]
        d = raw[0] * s[0] + raw[1] * s[1] + raw[2] * s[2]
        tp = [raw[c] - d * s[c] for c in range(3)]
        for c in range(3):
            tp_ref[image, c, here] = tp[c]
        pf = [pf_ref[image, c, here] for c in range(3)]
        acc_ref[0] += fold(tp[0] * tp[0] + tp[1] * tp[1] + tp[2] * tp[2])
        acc_ref[1] += fold(pf[0] * tp[0] + pf[1] * tp[1] + pf[2] * tp[2])
        acc_ref[2] += fold(fwd[0] * fwd[0] + fwd[1] * fwd[1] + fwd[2] * fwd[2])
        acc_ref[3] += fold(bwd[0] * bwd[0] + bwd[1] * bwd[1] + bwd[2] * bwd[2])

    for parity, refs in ((True, (first_ref, second_ref)), (False, (second_ref, first_ref))):
        for mode, chosen in ((1, up > 0), (-1, up < 0), (0, up == 0)):
            pl.when((even == parity) & chosen)(functools.partial(body, *refs, mode))

    @pl.when(step == pl.num_programs(1) - 1)
    def _():
        lane = lax.broadcasted_iota(jnp.int32, (8, 128), 1)
        row = lax.broadcasted_iota(jnp.int32, (8, 128), 0)
        out = jnp.zeros((8, 128), jnp.float32)
        for k in range(4):
            total = jnp.sum(acc_ref[k], keepdims=True)
            out = jnp.where((row == 0) & (lane == k), total, out)
        sums_ref[0] = out


def update_kernel(root_cells, rows, last, climber_ref, sums_ref, s_ref, v_ref, pf_ref, tp_ref, ns_ref, nv_ref, sp_ref):
    image = pl.program_id(0)
    here = pl.ds(pl.multiple_of(pl.program_id(1) * rows, rows), rows)
    tot = sums_ref[0]
    lane = lax.broadcasted_iota(jnp.int32, (8, 128), 1)
    row = lax.broadcasted_iota(jnp.int32, (8, 128), 0)

    def pick(k):
        return jnp.sum(jnp.where((row == 0) & (lane == k), tot, 0.0), keepdims=True)

    norm_t, along_t, next_sq, prev_sq = (pick(k) for k in range(4))
    scale = 1.0 / jnp.sqrt(norm_t + EPSILON)
    along = along_t * scale
    dist_next = jnp.sqrt(next_sq + EPSILON)
    dist_prev = jnp.sqrt(prev_sq + EPSILON)
    index = lax.axis_index("img") * pl.num_programs(0) + image
    climbing = jnp.full((1, 1), index) == climber_ref[0]
    ending = (jnp.full((1, 1), index) == 0) | (jnp.full((1, 1), index) == last)
    weight = jnp.where(climbing, 2.0 * along, along - SPRING * (dist_next - dist_prev))
    coef = jnp.where(ending, 0.0, weight * scale)
    keep = jnp.where(ending, 0.0, 1.0)

    @pl.when(pl.program_id(1) == 0)
    def _():
        pair = lax.broadcasted_iota(jnp.int32, (1, 2), 1)
        sp_ref[0] = jnp.where(pair == 0, dist_next, dist_prev) / root_cells

    f = [keep * pf_ref[image, c, here] - coef * tp_ref[image, c, here] for c in range(3)]
    v = [v_ref[image, c, here] for c in range(3)]
    vf = v[0] * f[0] + v[1] * f[1] + v[2] * f[2]
    ff = f[0] * f[0] + f[1] * f[1] + f[2] * f[2]
    gain = jnp.maximum(vf, 0.0) / jnp.maximum(ff, 1.0)
    nv = [gain * f[c] + TIME_STEP * f[c] for c in range(3)]
    moved = [s_ref[image, c, here] + TIME_STEP * nv[c] for c in range(3)]
    inverse = lax.rsqrt(moved[0] * moved[0] + moved[1] * moved[1] + moved[2] * moved[2])
    for c in range(3):
        nv_ref[0, c] = nv[c]
        ns_ref[0, c] = moved[c] * inverse


def per_device(spins, velocity, upwind, climber, coupling):
    count, _, nx, ny, nz = spins.shape
    total = count * lax.axis_size("img")
    cells = nx * ny * nz * lax.axis_size("gx") * lax.axis_size("gy")
    root_cells = float(cells) ** 0.5
    indices = lax.axis_index("img") * count + jnp.arange(count, dtype=jnp.int32)
    assert count == 1
    places = lax.axis_size("img")
    first = lax.ppermute(spins, "img", [(i, i ^ 1) for i in range(places) if i ^ 1 < places])
    second = lax.ppermute(
        spins, "img", [(i, i - 1 + 2 * (i % 2)) for i in range(1, places - 1)]
    )
    field = lattice_field(spins, coupling)
    perp_field = field - cell_dot(field, spins) * spins

    rows = ROWS if nx % ROWS == 0 else nx
    grid = (count, nx // rows)
    block = pl.BlockSpec((1, 3, rows, ny, nz), lambda i, j: (i, 0, j, 0, 0))
    small = pl.BlockSpec((1, 8, 128), lambda i, j: (i, 0, 0))
    smem = pl.BlockSpec(memory_space=pltpu.SMEM)
    whole = pl.BlockSpec(memory_space=pltpu.VMEM)
    params = pltpu.CompilerParams(
        dimension_semantics=("arbitrary", "arbitrary"), vmem_limit_bytes=VMEM_LIMIT
    )
    big = jax.ShapeDtypeStruct(spins.shape, jnp.float32)
    nbytes = spins.size * 4
    rows_a = ROWS_A if nx % ROWS_A == 0 else nx
    tangent_perp, sums = pl.pallas_call(
        functools.partial(tangent_kernel, rows_a),
        grid=(count, nx // rows_a),
        in_specs=[smem, whole, whole, whole, whole, whole],
        out_specs=[whole, small],
        out_shape=[big, jax.ShapeDtypeStruct((count, 8, 128), jnp.float32)],
        scratch_shapes=[pltpu.VMEM((4, 8, nz), jnp.float32)],
        compiler_params=params,
        cost_estimate=pl.CostEstimate(flops=40 * spins.size, bytes_accessed=5 * nbytes, transcendentals=0),
    )(upwind, spins, first, second, perp_field, velocity)

    sums = group_sum(sums, ("gy", "gx"))
    new_spins, new_velocity, spacing = pl.pallas_call(
        functools.partial(update_kernel, root_cells, rows, total - 1),
        grid=grid,
        in_specs=[smem, small, whole, whole, whole, whole],
        out_specs=[block, block, pl.BlockSpec((1, 1, 2), lambda i, j: (i, 0, 0))],
        out_shape=[big, big, jax.ShapeDtypeStruct((count, 1, 2), jnp.float32)],
        compiler_params=params,
        cost_estimate=pl.CostEstimate(flops=45 * spins.size, bytes_accessed=6 * nbytes, transcendentals=spins.size // 3),
    )(climber, sums, spins, velocity, perp_field, tangent_perp)
    return new_spins, new_velocity, spacing.reshape(count, 2)


def solution(mesh):
    return jax.shard_map(
        per_device,
        mesh=mesh,
        in_specs=(
            P("img", None, "gx", "gy", None),
            P("img", None, "gx", "gy", None),
            P("img"),
            P(),
            P(),
        ),
        out_specs=(
            P("img", None, "gx", "gy", None),
            P("img", None, "gx", "gy", None),
            P("img", None),
        ),
        check_vma=False,
    )
```
